512 devices in a mesh: region: 8 (over z), sub: 64 (over y, x, core).
Axes of the slice: x: 4, y: 8, z: 8, core: 2. Of those that a mesh axis runs over, the one named last changes fastest.
Arguments:
- right_side: bfloat16 [8, 64, 1024, 256], P('region', 'sub'), may hold values from -6 to 6
- local_inverse: bfloat16 [8, 64, 1024, 1024], P('region', 'sub')
- coupling: bfloat16 [8, 64, 4, 256, 256], P('region', 'sub'), may hold values from -0.75 to 0.75
- margin_blocks: int32 [4, 8, 64, 2], P(None, 'region', 'sub'), may hold values from 0 to 7, as said below
- partner: int32 [4, 512], replicated, may hold values from 0 to 511, as said below
- restriction: bfloat16 [8, 64, 64, 1024], P('region', 'sub'), may hold values from -0.375 to 0.375
- coarse_rows: bfloat16 [8, 4096, 4096], P('region', 'sub')
Outputs:
- solution: bfloat16 [8, 64, 1024, 256], P('region', 'sub')
The draws below stay inside these ranges and needn't reach their ends.
Inputs may be any that keep to these rules, and one draw needn't show every extreme that they name: `margin_blocks`: for each colour, subdomain and k, a block number below 8; the 2 numbers of one colour and subdomain are distinct. For each colour a perfect matching of all subdomains: the partner of a subdomain's partner is the subdomain itself, and no subdomain is its own partner.
All inputs are finite; a program needn't handle non-finite values.
Results may differ from the reference program's by a relative error of at most 0.0052.
Values may be sent and summed in bfloat16 or wider, within the bound.
No kernel may reach another device: no remote copies, remote signals or barrier semaphores. Data moves between devices by JAX's collectives and lax.ppermute only.
A program may use at most 64 MiB of HBM per device.

```python
import jax
import jax.numpy as jnp
from jax import lax

SUB_ROWS = 1024
NRHS = 256
BLK = 128
OVL_BLK = 2
COLORS = 4
CP = 64
REGIONS = 8
SUBS = 64
OVL = 256


def dominant_square(key, leading, order, scale_low, scale_high):

    def one_slab(index):
        slab_key = jax.random.fold_in(key, index)
        first_key, second_key = jax.random.split(slab_key)
        scatter_part = jax.random.normal(first_key, leading[1:] + (order, order), jnp.float32) * (0.7 / jnp.sqrt(jnp.float32(order)))
        diagonal_part = jax.random.uniform(second_key, leading[1:] + (order,), jnp.float32, scale_low, scale_high)
        return scatter_part + jnp.eye(order, dtype=jnp.float32) * diagonal_part[..., None, :]
    return lax.map(one_slab, jnp.arange(leading[0], dtype=jnp.int32))


def draw_local_inverse(key, part):
    return dominant_square(jax.random.fold_in(key, 11), (REGIONS, SUBS), SUB_ROWS, 1.0, 2.0).astype(jnp.bfloat16)


def draw_coarse_rows(key, part):
    return dominant_square(jax.random.fold_in(key, 23), (REGIONS,), SUBS * CP, 1.0, 2.0).astype(jnp.bfloat16)


def draw_margin_blocks(key, part):
    block_count = SUB_ROWS // BLK
    scores = jax.random.randint(jax.random.fold_in(key, 37), (COLORS, REGIONS, SUBS, block_count), 0, 1 << 20)
    scores = scores * block_count + jnp.arange(block_count, dtype=jnp.int32)
    ordered = jnp.argsort(scores, axis=-1, stable=True).astype(jnp.int32)
    return ordered[..., :OVL_BLK]


def matching(key, members):
    shuffled = jax.random.permutation(key, members).astype(jnp.int32)
    paired = shuffled.reshape(members // 2, 2)
    mates = jnp.zeros((members,), jnp.int32)
    mates = mates.at[paired[:, 0]].set(paired[:, 1])
    return mates.at[paired[:, 1]].set(paired[:, 0])


def draw_partner(key, part):
    colour_keys = jax.random.split(jax.random.fold_in(key, 41), COLORS)
    return jax.vmap(lambda single: matching(single, REGIONS * SUBS))(colour_keys)


def steps_of(rng, dims, cuts, smallest, largest):
    factor_of = 1.0
    for axis_at, parts in cuts:
        steps = jax.random.uniform(jax.random.fold_in(jax.random.fold_in(rng, 6), axis_at), (parts,), jnp.float32, smallest / len(cuts), largest / len(cuts))
        factor_of = factor_of * jnp.repeat(jnp.exp(steps), dims[axis_at] // parts).reshape((-1,) + (1,) * (len(dims) - 1 - axis_at))
    return factor_of


def noise(own_key, dims, scale, limit, pieces=(), held_as=jnp.bfloat16):
    result = scale * jax.random.normal(own_key, dims, jnp.float32)
    if pieces:
        result = result * steps_of(own_key, dims, pieces, -0.22, 0.18)
    return jnp.clip(result, -limit, limit).astype(held_as)


def setup_inputs(seed: int = 0) -> dict:
    key_list = jax.random.split(jax.random.key(seed), 8)
    right_side = noise(key_list[0], (REGIONS, SUBS, SUB_ROWS, NRHS), 1.0, 6.0, ((0, 8), (1, 64)))
    local_inverse = draw_local_inverse(jax.random.fold_in(key_list[7], 71), 0)
    coupling = noise(key_list[2], (REGIONS, SUBS, COLORS, OVL, OVL), (OVL // 4) ** -0.5, 0.75, ((0, 8), (1, 64)))
    margin_blocks = draw_margin_blocks(jax.random.fold_in(key_list[7], 71), 0)
    partner = draw_partner(jax.random.fold_in(key_list[7], 71), 0)
    restriction = noise(key_list[5], (REGIONS, SUBS, CP, SUB_ROWS), (SUB_ROWS // 4) ** -0.5, 0.375, ((0, 8), (1, 64)))
    coarse_rows = draw_coarse_rows(jax.random.fold_in(key_list[7], 71), 0)
    return dict(right_side=right_side, local_inverse=local_inverse, coupling=coupling, margin_blocks=margin_blocks, partner=partner, restriction=restriction, coarse_rows=coarse_rows)


def region_product(inputs_pair):
    return jnp.einsum("sab,sbn->san", inputs_pair[0].astype(jnp.float32), inputs_pair[1].astype(jnp.float32))


def coarse_product(inputs_pair):
    return jnp.dot(inputs_pair[0].astype(jnp.float32), inputs_pair[1].astype(jnp.float32)).astype(jnp.bfloat16)


def reference(right_side, local_inverse, coupling, margin_blocks, partner, restriction, coarse_rows):
    block_count = SUB_ROWS // BLK
    residual = right_side.astype(jnp.float32)
    accumulated = jnp.zeros(residual.shape, jnp.float32)
    for colour in range(COLORS):
        picked = margin_blocks[colour]
        tiled = residual.reshape(REGIONS, SUBS, block_count, BLK, NRHS)
        sent_rows = jnp.take_along_axis(tiled, picked[:, :, :, None, None], axis=2)
        sent_rows = sent_rows.reshape(REGIONS * SUBS, OVL, NRHS).astype(jnp.bfloat16)
        received = jnp.take(sent_rows, partner[colour], axis=0).reshape(REGIONS, SUBS, OVL, NRHS)
        coupled = jnp.einsum("gsab,gsbn->gsan", coupling[:, :, colour].astype(jnp.float32), received.astype(jnp.float32))
        one_hot = (picked[..., None] == jnp.arange(block_count, dtype=jnp.int32)).astype(jnp.float32)
        added = jnp.einsum("gskb,gskin->gsbin", one_hot, coupled.reshape(REGIONS, SUBS, OVL_BLK, BLK, NRHS))
        widened = residual + added.reshape(REGIONS, SUBS, SUB_ROWS, NRHS)
        shaped = widened.astype(jnp.bfloat16)
        correction = lax.map(region_product, (local_inverse, shaped))
        accumulated = accumulated + correction
        residual = widened - 0.25 * correction
    settled = residual.astype(jnp.bfloat16)
    projected = jnp.einsum("gscr,gsrn->gscn", restriction.astype(jnp.float32), settled.astype(jnp.float32)).astype(jnp.bfloat16)
    stacked = projected.reshape(REGIONS, SUBS * CP, NRHS)
    coarse = lax.map(coarse_product, (coarse_rows, stacked)).reshape(REGIONS, SUBS, CP, NRHS)
    lifted = jnp.einsum("gscr,gscn->gsrn", restriction.astype(jnp.float32), coarse.astype(jnp.float32))
    return (accumulated + lifted).astype(jnp.bfloat16)
```

```python
import jax
import jax.numpy as jnp
from jax import lax
from jax.sharding import PartitionSpec as P

BLK = 128
OVL_BLK = 2
COLORS = 4


def shards(right_side, local_inverse, coupling, margin_blocks, partner, restriction, coarse_rows):
    inverse = local_inverse[0, 0]
    tile_set = coupling[0, 0]
    own_blocks = margin_blocks[:, 0, 0, :]
    row_count = inverse.shape[0]
    columns = right_side.shape[-1]
    block_count = row_count // BLK
    span_rows = tile_set.shape[-1]
    sub_peers = lax.axis_size("sub")
    region_peers = lax.axis_size("region")
    all_peers = sub_peers * region_peers
    piece_len = span_rows * columns // all_peers
    residual = right_side[0, 0].astype(jnp.float32)
    accumulated = jnp.zeros(residual.shape, jnp.float32)
    block_ids = jnp.arange(block_count, dtype=jnp.int32)
    for colour in range(COLORS):
        picked = own_blocks[colour]
        tiled = residual.reshape(block_count, BLK, columns)
        sent_rows = jnp.take(tiled, picked, axis=0).reshape(span_rows, columns).astype(jnp.bfloat16)
        pieces = sent_rows.reshape(all_peers, piece_len)
        relayed = lax.all_to_all(pieces, ("region", "sub"), 0, 0, tiled=True)
        relayed = jnp.take(relayed, partner[colour], axis=0)
        returned = lax.all_to_all(relayed, ("region", "sub"), 0, 0, tiled=True)
        received = returned.reshape(span_rows, columns)
        coupled = jnp.dot(tile_set[colour], received, preferred_element_type=jnp.float32)
        one_hot = (picked[:, None] == block_ids[None, :]).astype(jnp.float32)
        added = jnp.einsum(
            "kb,kin->bin",
            one_hot,
            coupled.reshape(OVL_BLK, BLK, columns),
            precision=lax.Precision.HIGHEST,
        )
        widened = residual + added.reshape(row_count, columns)
        shaped = widened.astype(jnp.bfloat16)
        correction = jnp.dot(inverse, shaped, preferred_element_type=jnp.float32)
        accumulated = accumulated + correction
        residual = widened - 0.25 * correction
    settled = residual.astype(jnp.bfloat16)
    own_restriction = restriction[0, 0]
    projected = jnp.dot(own_restriction, settled, preferred_element_type=jnp.float32).astype(
        jnp.bfloat16
    )
    own_rows = coarse_rows[0]
    copies = jnp.broadcast_to(projected[None], (sub_peers,) + projected.shape)
    gathered = lax.all_to_all(copies, "sub", 0, 0, tiled=True).reshape(-1, columns)
    coarse = jnp.dot(
        own_rows,
        gathered,
        preferred_element_type=jnp.float32,
    ).astype(jnp.bfloat16)
    lifted = lax.dot_general(
        own_restriction, coarse, (((0,), (0,)), ((), ())), preferred_element_type=jnp.float32
    )
    return (accumulated + lifted).astype(jnp.bfloat16)[None, None]


def solution(mesh):
    placed = (
        P("region", "sub", None, None),
        P("region", "sub", None, None),
        P("region", "sub", None, None, None),
        P(None, "region", "sub", None),
        P(),
        P("region", "sub", None, None),
        P("region", "sub", None),
    )
    return jax.shard_map(
        shards,
        mesh=mesh,
        in_specs=placed,
        out_specs=P("region", "sub", None, None),
        check_vma=False,
    )
```

```python
import jax
import jax.numpy as jnp
from jax import lax
from jax.sharding import PartitionSpec as P

BLK = 128
OVL_BLK = 2
COLORS = 4


def rows_of(matrix, picked):
    return jnp.concatenate(
        [lax.dynamic_slice_in_dim(matrix, picked[k] * BLK, BLK, axis=0) for k in range(OVL_BLK)],
        axis=0,
    )


def exchange(sent_rows, mates, all_peers):
    span_rows, columns = sent_rows.shape
    pieces = sent_rows.reshape(all_peers, span_rows * columns // all_peers)
    relayed = lax.all_to_all(pieces, ("region", "sub"), 0, 0, tiled=True)
    relayed = jnp.take(relayed, mates, axis=0)
    returned = lax.all_to_all(relayed, ("region", "sub"), 0, 0, tiled=True)
    return returned.reshape(span_rows, columns)


def shards(right_side, local_inverse, coupling, margin_blocks, partner, restriction, coarse_rows):
    inverse = local_inverse[0, 0]
    tile_set = coupling[0, 0]
    own_blocks = margin_blocks[:, 0, 0, :]
    columns = right_side.shape[-1]
    sub_peers = lax.axis_size("sub")
    all_peers = sub_peers * lax.axis_size("region")
    residual = right_side[0, 0].astype(jnp.float32)
    accumulated = None
    sent_rows = rows_of(right_side[0, 0], own_blocks[0])
    for colour in range(COLORS):
        picked = own_blocks[colour]
        received = exchange(sent_rows, partner[colour], all_peers)
        coupled = jnp.dot(tile_set[colour], received, preferred_element_type=jnp.float32)
        widened = residual
        for k in range(OVL_BLK):
            start = picked[k] * BLK
            block = lax.dynamic_slice_in_dim(widened, start, BLK, axis=0)
            widened = lax.dynamic_update_slice_in_dim(
                widened, block + coupled[k * BLK:(k + 1) * BLK], start, axis=0
            )
        shaped = widened.astype(jnp.bfloat16)
        if colour + 1 < COLORS:
            upcoming = own_blocks[colour + 1]
            ahead = jnp.dot(rows_of(inverse, upcoming), shaped, preferred_element_type=jnp.float32)
            sent_rows = (rows_of(widened, upcoming) - 0.25 * ahead).astype(jnp.bfloat16)
        correction = jnp.dot(inverse, shaped, preferred_element_type=jnp.float32)
        accumulated = correction if accumulated is None else accumulated + correction
        residual = widened - 0.25 * correction
    settled = residual.astype(jnp.bfloat16)
    own_restriction = restriction[0, 0]
    projected = jnp.dot(own_restriction, settled, preferred_element_type=jnp.float32).astype(
        jnp.bfloat16
    )
    copies = jnp.broadcast_to(projected[None], (sub_peers,) + projected.shape)
    gathered = lax.all_to_all(copies, "sub", 0, 0, tiled=True).reshape(-1, columns)
    coarse = jnp.dot(coarse_rows[0], gathered, preferred_element_type=jnp.float32).astype(
        jnp.bfloat16
    )
    lifted = lax.dot_general(
        own_restriction, coarse, (((0,), (0,)), ((), ())), preferred_element_type=jnp.float32
    )
    return (accumulated + lifted).astype(jnp.bfloat16)[None, None]


def solution(mesh):
    placed = (
        P("region", "sub", None, None),
        P("region", "sub", None, None),
        P("region", "sub", None, None, None),
        P(None, "region", "sub", None),
        P(),
        P("region", "sub", None, None),
        P("region", "sub", None),
    )
    return jax.shard_map(
        shards,
        mesh=mesh,
        in_specs=placed,
        out_specs=P("region", "sub", None, None),
        check_vma=False,
    )
```

```python
import jax
import jax.numpy as jnp
from jax import lax
from jax.sharding import PartitionSpec as P

BLK = 128
OVL_BLK = 2
COLORS = 4


def rows_of(matrix, picked):
    return jnp.concatenate(
        [lax.dynamic_slice_in_dim(matrix, picked[k] * BLK, BLK, axis=0) for k in range(OVL_BLK)],
        axis=0,
    )


def exchange(sent_rows, mates, all_peers):
    span_rows, columns = sent_rows.shape
    pieces = sent_rows.reshape(all_peers, span_rows * columns // all_peers)
    relayed = lax.all_to_all(pieces, ("region", "sub"), 0, 0, tiled=True)
    relayed = jnp.take(relayed, mates, axis=0)
    returned = lax.all_to_all(relayed, ("region", "sub"), 0, 0, tiled=True)
    return returned.reshape(span_rows, columns)


def shards(right_side, local_inverse, coupling, margin_blocks, partner, restriction, coarse_rows):
    inverse = local_inverse[0, 0]
    tile_set = coupling[0, 0]
    own_blocks = margin_blocks[:, 0, 0, :]
    columns = right_side.shape[-1]
    sub_peers = lax.axis_size("sub")
    all_peers = sub_peers * lax.axis_size("region")
    residual = right_side[0, 0].astype(jnp.float32)
    accumulated = None
    sent_rows = rows_of(right_side[0, 0], own_blocks[0])
    for colour in range(COLORS):
        picked = own_blocks[colour]
        received = exchange(sent_rows, partner[colour], all_peers)
        base = residual.astype(jnp.bfloat16)
        if colour + 1 < COLORS:
            next_inverse_rows = rows_of(inverse, own_blocks[colour + 1])
            next_residual_rows = rows_of(residual, own_blocks[colour + 1])
        coupled = jnp.dot(tile_set[colour], received, preferred_element_type=jnp.float32)
        parts = [coupled[k * BLK:(k + 1) * BLK] for k in range(OVL_BLK)]
        widened = residual
        shaped = base
        for k in range(OVL_BLK):
            start = picked[k] * BLK
            block = lax.dynamic_slice_in_dim(residual, start, BLK, axis=0) + parts[k]
            widened = lax.dynamic_update_slice_in_dim(widened, block, start, axis=0)
            shaped = lax.dynamic_update_slice_in_dim(shaped, block.astype(jnp.bfloat16), start, axis=0)
        if colour + 1 < COLORS:
            upcoming = own_blocks[colour + 1]
            ahead = jnp.dot(next_inverse_rows, shaped, preferred_element_type=jnp.float32)
            near = []
            for j in range(OVL_BLK):
                row = next_residual_rows[j * BLK:(j + 1) * BLK]
                for k in range(OVL_BLK):
                    row = jnp.where(upcoming[j] == picked[k], row + parts[k], row)
                near.append(row)
            sent_rows = (jnp.concatenate(near, axis=0) - 0.25 * ahead).astype(jnp.bfloat16)
        correction = jnp.dot(inverse, shaped, preferred_element_type=jnp.float32)
        accumulated = correction if accumulated is None else accumulated + correction
        residual = widened - 0.25 * correction
    settled = residual.astype(jnp.bfloat16)
    own_restriction = restriction[0, 0]
    projected = jnp.dot(own_restriction, settled, preferred_element_type=jnp.float32).astype(
        jnp.bfloat16
    )
    copies = jnp.broadcast_to(projected[None], (sub_peers,) + projected.shape)
    gathered = lax.all_to_all(copies, "sub", 0, 0, tiled=True).reshape(-1, columns)
    coarse = jnp.dot(coarse_rows[0], gathered, preferred_element_type=jnp.float32).astype(
        jnp.bfloat16
    )
    lifted = lax.dot_general(
        own_restriction, coarse, (((0,), (0,)), ((), ())), preferred_element_type=jnp.float32
    )
    return (accumulated + lifted).astype(jnp.bfloat16)[None, None]


def solution(mesh):
    placed = (
        P("region", "sub", None, None),
        P("region", "sub", None, None),
        P("region", "sub", None, None, None),
        P(None, "region", "sub", None),
        P(),
        P("region", "sub", None, None),
        P("region", "sub", None),
    )
    return jax.shard_map(
        shards,
        mesh=mesh,
        in_specs=placed,
        out_specs=P("region", "sub", None, None),
        check_vma=False,
    )
```

```python
import jax
import jax.numpy as jnp
from jax import lax
from jax.experimental import pallas as pl
from jax.sharding import PartitionSpec as P

BLK = 128
OVL_BLK = 2
COLORS = 4
ROW_TILE = 256


def _update_kernel(inverse_ref, shaped_ref, widened_ref, accumulated_ref, accumulated_out, residual_out):
    correction = jnp.dot(inverse_ref[...], shaped_ref[...], preferred_element_type=jnp.float32)
    accumulated_out[...] = accumulated_ref[...] + correction
    residual_out[...] = widened_ref[...] - 0.25 * correction


def _first_kernel(inverse_ref, shaped_ref, widened_ref, accumulated_out, residual_out):
    correction = jnp.dot(inverse_ref[...], shaped_ref[...], preferred_element_type=jnp.float32)
    accumulated_out[...] = correction
    residual_out[...] = widened_ref[...] - 0.25 * correction


def local_update(inverse, shaped, widened, accumulated):
    rows, columns = widened.shape
    steps = rows // ROW_TILE
    tile = pl.BlockSpec((ROW_TILE, columns), lambda i: (i, 0))
    specs = [
        pl.BlockSpec((ROW_TILE, rows), lambda i: (i, 0)),
        pl.BlockSpec((rows, columns), lambda i: (0, 0)),
        tile,
    ]
    operands = [inverse, shaped, widened]
    if accumulated is None:
        kernel = _first_kernel
    else:
        kernel = _update_kernel
        specs.append(tile)
        operands.append(accumulated)
    out = jax.ShapeDtypeStruct((rows, columns), jnp.float32)
    cost = pl.CostEstimate(
        flops=2 * rows * rows * columns,
        transcendentals=0,
        bytes_accessed=rows * rows * 2 + rows * columns * 2 + rows * columns * 4 * len(operands),
    )
    return pl.pallas_call(
        kernel,
        out_shape=(out, out),
        grid=(steps,),
        in_specs=specs,
        out_specs=(tile, tile),
        cost_estimate=cost,
    )(*operands)


def rows_of(matrix, picked):
    return jnp.concatenate(
        [lax.dynamic_slice_in_dim(matrix, picked[k] * BLK, BLK, axis=0) for k in range(OVL_BLK)],
        axis=0,
    )


def exchange(sent_rows, mates, all_peers):
    span_rows, columns = sent_rows.shape
    pieces = sent_rows.reshape(all_peers, span_rows * columns // all_peers)
    relayed = lax.all_to_all(pieces, ("region", "sub"), 0, 0, tiled=True)
    relayed = jnp.take(relayed, mates, axis=0)
    returned = lax.all_to_all(relayed, ("region", "sub"), 0, 0, tiled=True)
    return returned.reshape(span_rows, columns)


def shards(right_side, local_inverse, coupling, margin_blocks, partner, restriction, coarse_rows):
    inverse = local_inverse[0, 0]
    tile_set = coupling[0, 0]
    own_blocks = margin_blocks[:, 0, 0, :]
    columns = right_side.shape[-1]
    sub_peers = lax.axis_size("sub")
    all_peers = sub_peers * lax.axis_size("region")
    residual = right_side[0, 0].astype(jnp.float32)
    accumulated = None
    sent_rows = rows_of(right_side[0, 0], own_blocks[0])
    for colour in range(COLORS):
        picked = own_blocks[colour]
        received = exchange(sent_rows, partner[colour], all_peers)
        coupled = jnp.dot(tile_set[colour], received, preferred_element_type=jnp.float32)
        widened = residual
        for k in range(OVL_BLK):
            start = picked[k] * BLK
            block = lax.dynamic_slice_in_dim(widened, start, BLK, axis=0)
            widened = lax.dynamic_update_slice_in_dim(
                widened, block + coupled[k * BLK:(k + 1) * BLK], start, axis=0
            )
        shaped = widened.astype(jnp.bfloat16)
        if colour + 1 < COLORS:
            upcoming = own_blocks[colour + 1]
            ahead = jnp.dot(rows_of(inverse, upcoming), shaped, preferred_element_type=jnp.float32)
            sent_rows = (rows_of(widened, upcoming) - 0.25 * ahead).astype(jnp.bfloat16)
        accumulated, residual = local_update(inverse, shaped, widened, accumulated)
    settled = residual.astype(jnp.bfloat16)
    own_restriction = restriction[0, 0]
    projected = jnp.dot(own_restriction, settled, preferred_element_type=jnp.float32).astype(
        jnp.bfloat16
    )
    copies = jnp.broadcast_to(projected[None], (sub_peers,) + projected.shape)
    gathered = lax.all_to_all(copies, "sub", 0, 0, tiled=True).reshape(-1, columns)
    coarse = jnp.dot(coarse_rows[0], gathered, preferred_element_type=jnp.float32).astype(
        jnp.bfloat16
    )
    lifted = lax.dot_general(
        own_restriction, coarse, (((0,), (0,)), ((), ())), preferred_element_type=jnp.float32
    )
    return (accumulated + lifted).astype(jnp.bfloat16)[None, None]


def solution(mesh):
    placed = (
        P("region", "sub", None, None),
        P("region", "sub", None, None),
        P("region", "sub", None, None, None),
        P(None, "region", "sub", None),
        P(),
        P("region", "sub", None, None),
        P("region", "sub", None),
    )
    return jax.shard_map(
        shards,
        mesh=mesh,
        in_specs=placed,
        out_specs=P("region", "sub", None, None),
        check_vma=False,
    )
```

```python
import jax
import jax.numpy as jnp
from jax import lax
from jax.experimental import pallas as pl
from jax.experimental.pallas import tpu as pltpu
from jax.sharding import PartitionSpec as P

BLK = 128
OVL_BLK = 2
COLORS = 4


def _update_body(picked_ref, inverse_ref, shaped_ref, residual_ref, coupled_ref, accumulated_ref, accumulated_out, residual_out, base_out):
    block = pl.program_id(0)
    correction = jnp.dot(inverse_ref[...], shaped_ref[...], preferred_element_type=jnp.float32)
    widened = residual_ref[...]
    for k in range(OVL_BLK):
        widened = jnp.where(picked_ref[k] == block, widened + coupled_ref[k * BLK:(k + 1) * BLK, :], widened)
    if accumulated_ref is None:
        accumulated_out[...] = correction
    else:
        accumulated_out[...] = accumulated_ref[...] + correction
    updated = widened - 0.25 * correction
    residual_out[...] = updated
    base_out[...] = updated.astype(jnp.bfloat16)


def _first_kernel(picked_ref, inverse_ref, shaped_ref, residual_ref, coupled_ref, accumulated_out, residual_out, base_out):
    _update_body(picked_ref, inverse_ref, shaped_ref, residual_ref, coupled_ref, None, accumulated_out, residual_out, base_out)


def local_update(picked, inverse, shaped, residual, coupled, accumulated):
    rows, columns = residual.shape
    tile = pl.BlockSpec((BLK, columns), lambda i, p: (i, 0))
    specs = [
        pl.BlockSpec((BLK, rows), lambda i, p: (i, 0)),
        pl.BlockSpec((rows, columns), lambda i, p: (0, 0)),
        tile,
        pl.BlockSpec(coupled.shape, lambda i, p: (0, 0)),
    ]
    operands = [inverse, shaped, residual, coupled]
    if accumulated is None:
        kernel = _first_kernel
    else:
        kernel = _update_body
        specs.append(tile)
        operands.append(accumulated)
    wide = jax.ShapeDtypeStruct((rows, columns), jnp.float32)
    narrow = jax.ShapeDtypeStruct((rows, columns), jnp.bfloat16)
    cost = pl.CostEstimate(
        flops=2 * rows * rows * columns,
        transcendentals=0,
        bytes_accessed=rows * rows * 2 + rows * columns * (2 + 4 * len(operands) + 2),
    )
    grid_spec = pltpu.PrefetchScalarGridSpec(
        num_scalar_prefetch=1,
        grid=(rows // BLK,),
        in_specs=specs,
        out_specs=(tile, tile, tile),
    )
    return pl.pallas_call(
        kernel,
        out_shape=(wide, wide, narrow),
        grid_spec=grid_spec,
        cost_estimate=cost,
    )(picked, *operands)


def rows_of(matrix, picked):
    return jnp.concatenate(
        [lax.dynamic_slice_in_dim(matrix, picked[k] * BLK, BLK, axis=0) for k in range(OVL_BLK)],
        axis=0,
    )


def exchange(sent_rows, mates, all_peers):
    span_rows, columns = sent_rows.shape
    pieces = sent_rows.reshape(all_peers, span_rows * columns // all_peers)
    relayed = lax.all_to_all(pieces, ("region", "sub"), 0, 0, tiled=True)
    relayed = jnp.take(relayed, mates, axis=0)
    returned = lax.all_to_all(relayed, ("region", "sub"), 0, 0, tiled=True)
    return returned.reshape(span_rows, columns)


def shards(right_side, local_inverse, coupling, margin_blocks, partner, restriction, coarse_rows):
    inverse = local_inverse[0, 0]
    tile_set = coupling[0, 0]
    own_blocks = margin_blocks[:, 0, 0, :]
    columns = right_side.shape[-1]
    sub_peers = lax.axis_size("sub")
    all_peers = sub_peers * lax.axis_size("region")
    base = right_side[0, 0]
    residual = base.astype(jnp.float32)
    accumulated = None
    sent_rows = rows_of(base, own_blocks[0])
    for colour in range(COLORS):
        picked = own_blocks[colour]
        received = exchange(sent_rows, partner[colour], all_peers)
        if colour + 1 < COLORS:
            upcoming = own_blocks[colour + 1]
            next_inverse_rows = rows_of(inverse, upcoming)
            next_residual_rows = rows_of(residual, upcoming)
        coupled = jnp.dot(tile_set[colour], received, preferred_element_type=jnp.float32)
        parts = [coupled[k * BLK:(k + 1) * BLK] for k in range(OVL_BLK)]
        shaped = base
        for k in range(OVL_BLK):
            start = picked[k] * BLK
            block = lax.dynamic_slice_in_dim(residual, start, BLK, axis=0) + parts[k]
            shaped = lax.dynamic_update_slice_in_dim(shaped, block.astype(jnp.bfloat16), start, axis=0)
        if colour + 1 < COLORS:
            ahead = jnp.dot(next_inverse_rows, shaped, preferred_element_type=jnp.float32)
            near = []
            for j in range(OVL_BLK):
                row = next_residual_rows[j * BLK:(j + 1) * BLK]
                for k in range(OVL_BLK):
                    row = jnp.where(upcoming[j] == picked[k], row + parts[k], row)
                near.append(row)
            sent_rows = (jnp.concatenate(near, axis=0) - 0.25 * ahead).astype(jnp.bfloat16)
        accumulated, residual, base = local_update(picked, inverse, shaped, residual, coupled, accumulated)
    own_restriction = restriction[0, 0]
    projected = jnp.dot(own_restriction, base, preferred_element_type=jnp.float32).astype(
        jnp.bfloat16
    )
    copies = jnp.broadcast_to(projected[None], (sub_peers,) + projected.shape)
    gathered = lax.all_to_all(copies, "sub", 0, 0, tiled=True).reshape(-1, columns)
    coarse = jnp.dot(coarse_rows[0], gathered, preferred_element_type=jnp.float32).astype(
        jnp.bfloat16
    )
    lifted = lax.dot_general(
        own_restriction, coarse, (((0,), (0,)), ((), ())), preferred_element_type=jnp.float32
    )
    return (accumulated + lifted).astype(jnp.bfloat16)[None, None]


def solution(mesh):
    placed = (
        P("region", "sub", None, None),
        P("region", "sub", None, None),
        P("region", "sub", None, None, None),
        P(None, "region", "sub", None),
        P(),
        P("region", "sub", None, None),
        P("region", "sub", None),
    )
    return jax.shard_map(
        shards,
        mesh=mesh,
        in_specs=placed,
        out_specs=P("region", "sub", None, None),
        check_vma=False,
    )
```

```python
import jax
import jax.numpy as jnp
from jax import lax
from jax.experimental import pallas as pl
from jax.sharding import PartitionSpec as P

BLK = 128
OVL_BLK = 2
COLORS = 4
ROW_TILE = 256


def _update_kernel(inverse_ref, shaped_ref, widened_ref, accumulated_ref, accumulated_out, residual_out):
    correction = jnp.dot(inverse_ref[...], shaped_ref[...], preferred_element_type=jnp.float32)
    accumulated_out[...] = accumulated_ref[...] + correction
    residual_out[...] = widened_ref[...] - 0.25 * correction


def _first_kernel(inverse_ref, shaped_ref, widened_ref, accumulated_out, residual_out):
    correction = jnp.dot(inverse_ref[...], shaped_ref[...], preferred_element_type=jnp.float32)
    accumulated_out[...] = correction
    residual_out[...] = widened_ref[...] - 0.25 * correction


def local_update(inverse, shaped, widened, accumulated):
    rows, columns = widened.shape
    steps = rows // ROW_TILE
    tile = pl.BlockSpec((ROW_TILE, columns), lambda i: (i, 0))
    specs = [
        pl.BlockSpec((ROW_TILE, rows), lambda i: (i, 0)),
        pl.BlockSpec((rows, columns), lambda i: (0, 0)),
        tile,
    ]
    operands = [inverse, shaped, widened]
    if accumulated is None:
        kernel = _first_kernel
    else:
        kernel = _update_kernel
        specs.append(tile)
        operands.append(accumulated)
    out = jax.ShapeDtypeStruct((rows, columns), jnp.float32)
    cost = pl.CostEstimate(
        flops=2 * rows * rows * columns,
        transcendentals=0,
        bytes_accessed=rows * rows * 2 + rows * columns * 2 + rows * columns * 4 * len(operands),
    )
    return pl.pallas_call(
        kernel,
        out_shape=(out, out),
        grid=(steps,),
        in_specs=specs,
        out_specs=(tile, tile),
        cost_estimate=cost,
    )(*operands)


def rows_of(matrix, picked):
    return jnp.concatenate(
        [lax.dynamic_slice_in_dim(matrix, picked[k] * BLK, BLK, axis=0) for k in range(OVL_BLK)],
        axis=0,
    )


def exchange(sent_rows, mates, all_peers):
    span_rows, columns = sent_rows.shape
    pieces = sent_rows.reshape(all_peers, span_rows * columns // all_peers)
    relayed = lax.all_to_all(pieces, ("region", "sub"), 0, 0, tiled=True)
    relayed = jnp.take(relayed, mates, axis=0)
    returned = lax.all_to_all(relayed, ("region", "sub"), 0, 0, tiled=True)
    return returned.reshape(span_rows, columns)


def shards(right_side, local_inverse, coupling, margin_blocks, partner, restriction, coarse_rows):
    inverse = local_inverse[0, 0]
    tile_set = coupling[0, 0]
    own_blocks = margin_blocks[:, 0, 0, :]
    columns = right_side.shape[-1]
    sub_peers = lax.axis_size("sub")
    all_peers = sub_peers * lax.axis_size("region")
    block_count = inverse.shape[0] // BLK
    residual = right_side[0, 0].astype(jnp.float32)
    accumulated = None
    sent_rows = rows_of(right_side[0, 0], own_blocks[0])
    for colour in range(COLORS):
        picked = own_blocks[colour]
        if colour + 1 < COLORS:
            next_inverse_rows = rows_of(inverse, own_blocks[colour + 1])
        received = exchange(sent_rows, partner[colour], all_peers)
        coupled = jnp.dot(tile_set[colour], received, preferred_element_type=jnp.float32)
        block_of_row = lax.broadcasted_iota(jnp.int32, (block_count, 1, 1), 0)
        added = jnp.zeros((block_count, BLK, columns), jnp.float32)
        for k in range(OVL_BLK):
            part = coupled[k * BLK:(k + 1) * BLK][None]
            added = jnp.where(block_of_row == picked[k], part, added)
        widened = residual + added.reshape(residual.shape)
        shaped = widened.astype(jnp.bfloat16)
        if colour + 1 < COLORS:
            upcoming = own_blocks[colour + 1]
            ahead = jnp.dot(next_inverse_rows, shaped, preferred_element_type=jnp.float32)
            sent_rows = (rows_of(widened, upcoming) - 0.25 * ahead).astype(jnp.bfloat16)
        accumulated, residual = local_update(inverse, shaped, widened, accumulated)
    settled = residual.astype(jnp.bfloat16)
    own_restriction = restriction[0, 0]
    projected = jnp.dot(own_restriction, settled, preferred_element_type=jnp.float32).astype(
        jnp.bfloat16
    )
    copies = jnp.broadcast_to(projected[None], (sub_peers,) + projected.shape)
    gathered = lax.all_to_all(copies, "sub", 0, 0, tiled=True).reshape(-1, columns)
    coarse = jnp.dot(coarse_rows[0], gathered, preferred_element_type=jnp.float32).astype(
        jnp.bfloat16
    )
    lifted = lax.dot_general(
        own_restriction, coarse, (((0,), (0,)), ((), ())), preferred_element_type=jnp.float32
    )
    return (accumulated + lifted).astype(jnp.bfloat16)[None, None]


def solution(mesh):
    placed = (
        P("region", "sub", None, None),
        P("region", "sub", None, None),
        P("region", "sub", None, None, None),
        P(None, "region", "sub", None),
        P(),
        P("region", "sub", None, None),
        P("region", "sub", None),
    )
    return jax.shard_map(
        shards,
        mesh=mesh,
        in_specs=placed,
        out_specs=P("region", "sub", None, None),
        check_vma=False,
    )
```

```python
import jax
import jax.numpy as jnp
from jax import lax
from jax.experimental import pallas as pl
from jax.sharding import PartitionSpec as P

BLK = 128
OVL_BLK = 2
COLORS = 4
ROW_TILE = 256


def _update_kernel(inverse_ref, shaped_ref, widened_ref, accumulated_ref, accumulated_out, residual_out):
    correction = jnp.dot(inverse_ref[...], shaped_ref[...], preferred_element_type=jnp.float32)
    accumulated_out[...] = accumulated_ref[...] + correction
    residual_out[...] = widened_ref[...] - 0.25 * correction


def _first_kernel(inverse_ref, shaped_ref, widened_ref, accumulated_out, residual_out):
    correction = jnp.dot(inverse_ref[...], shaped_ref[...], preferred_element_type=jnp.float32)
    accumulated_out[...] = correction
    residual_out[...] = widened_ref[...] - 0.25 * correction


def local_update(inverse, shaped, widened, accumulated):
    rows, columns = widened.shape
    steps = rows // ROW_TILE
    tile = pl.BlockSpec((ROW_TILE, columns), lambda i: (i, 0))
    specs = [
        pl.BlockSpec((ROW_TILE, rows), lambda i: (i, 0)),
        pl.BlockSpec((rows, columns), lambda i: (0, 0)),
        tile,
    ]
    operands = [inverse, shaped, widened]
    if accumulated is None:
        kernel = _first_kernel
    else:
        kernel = _update_kernel
        specs.append(tile)
        operands.append(accumulated)
    out = jax.ShapeDtypeStruct((rows, columns), jnp.float32)
    cost = pl.CostEstimate(
        flops=2 * rows * rows * columns,
        transcendentals=0,
        bytes_accessed=rows * rows * 2 + rows * columns * 2 + rows * columns * 4 * len(operands),
    )
    return pl.pallas_call(
        kernel,
        out_shape=(out, out),
        grid=(steps,),
        in_specs=specs,
        out_specs=(tile, tile),
        cost_estimate=cost,
    )(*operands)


def rows_of(matrix, picked):
    return jnp.concatenate(
        [lax.dynamic_slice_in_dim(matrix, picked[k] * BLK, BLK, axis=0) for k in range(OVL_BLK)],
        axis=0,
    )


def exchange(sent_rows, mates, all_peers):
    span_rows, columns = sent_rows.shape
    pieces = sent_rows.reshape(all_peers, span_rows * columns // all_peers)
    relayed = lax.all_to_all(pieces, ("region", "sub"), 0, 0, tiled=True)
    relayed = jnp.take(relayed, mates, axis=0)
    returned = lax.all_to_all(relayed, ("region", "sub"), 0, 0, tiled=True)
    return returned.reshape(span_rows, columns)


def gather_rows(block, peers):
    bits = peers.bit_length() - 1
    me = lax.axis_index("sub")
    held = block[None]
    for bit in reversed(range(bits)):
        other = lax.ppermute(held, "sub", [(i, i ^ (1 << bit)) for i in range(peers)])
        low = (me >> bit) & 1 == 0
        held = jnp.stack([jnp.where(low, held, other), jnp.where(low, other, held)], axis=0)
    held = held.reshape((2,) * bits + block.shape)
    held = jnp.transpose(held, tuple(reversed(range(bits))) + (bits, bits + 1))
    return held.reshape(peers * block.shape[0], block.shape[1])


def shards(right_side, local_inverse, coupling, margin_blocks, partner, restriction, coarse_rows):
    inverse = local_inverse[0, 0]
    tile_set = coupling[0, 0]
    own_blocks = margin_blocks[:, 0, 0, :]
    columns = right_side.shape[-1]
    sub_peers = lax.axis_size("sub")
    all_peers = sub_peers * lax.axis_size("region")
    block_count = inverse.shape[0] // BLK
    residual = right_side[0, 0].astype(jnp.float32)
    accumulated = None
    sent_rows = rows_of(right_side[0, 0], own_blocks[0])
    for colour in range(COLORS):
        picked = own_blocks[colour]
        if colour + 1 < COLORS:
            next_inverse_rows = rows_of(inverse, own_blocks[colour + 1])
        received = exchange(sent_rows, partner[colour], all_peers)
        coupled = jnp.dot(tile_set[colour], received, preferred_element_type=jnp.float32)
        block_of_row = lax.broadcasted_iota(jnp.int32, (block_count, 1, 1), 0)
        added = jnp.zeros((block_count, BLK, columns), jnp.float32)
        for k in range(OVL_BLK):
            part = coupled[k * BLK:(k + 1) * BLK][None]
            added = jnp.where(block_of_row == picked[k], part, added)
        widened = residual + added.reshape(residual.shape)
        shaped = widened.astype(jnp.bfloat16)
        if colour + 1 < COLORS:
            upcoming = own_blocks[colour + 1]
            ahead = jnp.dot(next_inverse_rows, shaped, preferred_element_type=jnp.float32)
            sent_rows = (rows_of(widened, upcoming) - 0.25 * ahead).astype(jnp.bfloat16)
        accumulated, residual = local_update(inverse, shaped, widened, accumulated)
    settled = residual.astype(jnp.bfloat16)
    own_restriction = restriction[0, 0]
    projected = jnp.dot(own_restriction, settled, preferred_element_type=jnp.float32).astype(
        jnp.bfloat16
    )
    gathered = gather_rows(projected, sub_peers)
    coarse = jnp.dot(coarse_rows[0], gathered, preferred_element_type=jnp.float32).astype(
        jnp.bfloat16
    )
    lifted = lax.dot_general(
        own_restriction, coarse, (((0,), (0,)), ((), ())), preferred_element_type=jnp.float32
    )
    return (accumulated + lifted).astype(jnp.bfloat16)[None, None]


def solution(mesh):
    placed = (
        P("region", "sub", None, None),
        P("region", "sub", None, None),
        P("region", "sub", None, None, None),
        P(None, "region", "sub", None),
        P(),
        P("region", "sub", None, None),
        P("region", "sub", None),
    )
    return jax.shard_map(
        shards,
        mesh=mesh,
        in_specs=placed,
        out_specs=P("region", "sub", None, None),
        check_vma=False,
    )
```
